256 devices in a mesh: gx: 16 (over y_lo, z), gy: 4 (over y_hi, core), gz: 4 (over x).
Axes of the slice: x: 4, y: 4 (y_hi: 2, y_lo: 2; y = y_hi * 2 + y_lo), z: 8, core: 2. Of those that a mesh axis runs over, the one named last changes fastest.
Arguments:
- velocity: float32 [3, 64, 32, 1024], P(None, 'gx', 'gy', 'gz'), may hold values from -6 to 6
- stress: float32 [6, 64, 32, 1024], P(None, 'gx', 'gy', 'gz'), may hold values from -6 to 6
- buoyancy: float32 [64, 32, 1024], P('gx', 'gy', 'gz'), may hold values from 0.5 to 1
- lame_lambda: float32 [64, 32, 1024], P('gx', 'gy', 'gz'), may hold values from 0.5 to 1.5
- shear_modulus: float32 [64, 32, 1024], P('gx', 'gy', 'gz'), may hold values from 0.3 to 1
- slip_rate: bfloat16 [2048, 4096], P(('gx', 'gy', 'gz')), may hold values from 0 to 2
- taps: bfloat16 [512], replicated, may hold values from -0.25 to 0.25
- moment: float32 [6, 2048], P(None, ('gx', 'gy', 'gz')), may hold values from -6 to 6
- cells: int32 [3, 2048], replicated, may hold values from 0 to 511, as said below
- onsets: int32 [2048], P(('gx', 'gy', 'gz')), may hold values from 0 to 2624, as said below
Outputs:
- velocity_out: float32 [3, 64, 32, 1024], P(None, 'gx', 'gy', 'gz')
- stress_out: float32 [6, 64, 32, 1024], P(None, 'gx', 'gy', 'gz')
The draws below stay inside these ranges and needn't reach their ends.
Inputs may be any that keep to these rules, and one draw needn't show every extreme that they name: `cells`: row 0 is below 64, row 1 is 15 or 16, row 2 is below 512. `onsets`: every subfault's frames lie inside its slip-rate function.
All inputs are finite; a program needn't handle non-finite values.
Results may differ from the reference program's by a relative error of at most 0.0003.
Values sent between devices are 32-bit elements; how exact they have to be, the bound alone decides.
No kernel may reach another device: no remote copies, remote signals or barrier semaphores. Data moves between devices by JAX's collectives and lax.ppermute only.
A program may use at most 64 MiB of HBM per device.

```python
import jax
import jax.numpy as jnp
from jax import lax

NS = 4096
TAPS = 512
HOP = 64
STEPS = 16
NX = 64
NY = 32
NZ = 1024
SUB = 2048


def draw_cells(key, part):
    key_x, key_y, key_z = jax.random.split(key, 3)
    strike = jax.random.randint(key_x, (SUB,), 0, NX)
    across = NY // 2 - 1 + jax.random.randint(key_y, (SUB,), 0, 2)
    downdip = jax.random.randint(key_z, (SUB,), 0, NZ // 2)
    strike = strike.at[0].set(NX - 1).at[1].set(0)
    across = across.at[0].set(NY // 2)
    downdip = downdip.at[0].set(NZ // 2 - 1).at[1].set(0)
    return jnp.stack([strike, across, downdip]).astype(jnp.int32)


def draw_onsets(key, part):
    latest = NS - TAPS - HOP * (STEPS - 1)
    values = jax.random.randint(key, (SUB,), 0, latest + 1)
    values = values.at[0].set(latest).at[1].set(0)
    return values.astype(jnp.int32)


def level_of(rng, dims, cuts, low, top_value):
    loudness = 1.0
    for axis_at, shards_of in cuts:
        steps = jax.random.uniform(jax.random.fold_in(jax.random.fold_in(rng, 6), axis_at), (shards_of,), jnp.float32, low / len(cuts), top_value / len(cuts))
        loudness = loudness * jnp.repeat(jnp.exp(steps), dims[axis_at] // shards_of).reshape((-1,) + (1,) * (len(dims) - 1 - axis_at))
    return loudness


def normal_values(rng, dims, spread, limit, cuts=(), kind=jnp.bfloat16):
    values = jax.random.normal(rng, dims, jnp.float32) * spread
    if len(cuts) > 0:
        values = level_of(rng, dims, cuts, -0.22, 0.18) * values
    return jnp.clip(values, min=-limit, max=limit).astype(kind)


def setup_inputs(seed: int = 0) -> dict:
    splits = jax.random.split(jax.random.key(seed), 11)
    return {
        "velocity": normal_values(splits[0], (3, NX, NY, NZ), 1.0, 6.0, ((1, 16), (2, 4), (3, 4)), jnp.float32),
        "stress": normal_values(splits[1], (6, NX, NY, NZ), 1.0, 6.0, ((1, 16), (2, 4), (3, 4)), jnp.float32),
        "buoyancy": jnp.clip(0.5 + 0.5 * jax.random.uniform(splits[2], (NX, NY, NZ), jnp.float32) ** level_of(splits[2], (NX, NY, NZ), ((0, 16), (1, 4), (2, 4)), -0.2, 0.2), 0.5, 1.0),
        "lame_lambda": jnp.clip(0.5 + 1.0 * jax.random.uniform(splits[3], (NX, NY, NZ), jnp.float32) ** level_of(splits[3], (NX, NY, NZ), ((0, 16), (1, 4), (2, 4)), -0.2, 0.2), 0.5, 1.5),
        "shear_modulus": jnp.clip(0.3 + 0.7 * jax.random.uniform(splits[4], (NX, NY, NZ), jnp.float32) ** level_of(splits[4], (NX, NY, NZ), ((0, 16), (1, 4), (2, 4)), -0.2, 0.2), 0.3, 1.0),
        "slip_rate": jnp.clip(2.0 * jax.random.uniform(splits[5], (SUB, NS), jnp.float32) ** level_of(splits[5], (SUB, NS), ((0, 256),), -0.2, 0.2), 0.0, 2.0).astype(jnp.bfloat16),
        "taps": normal_values(splits[6], (TAPS,), TAPS ** -0.5, 0.25),
        "moment": normal_values(splits[7], (6, SUB), 1.0, 6.0, ((1, 256),), jnp.float32),
        "cells": draw_cells(jax.random.fold_in(splits[10], 71), 0),
        "onsets": draw_onsets(jax.random.fold_in(splits[10], 71), 0),
    }


STEP_TIME = 0.25


def window(array, axis, offset):
    cuts = [slice(None)] * (array.ndim - 3)
    for dim in range(3):
        extent = array.shape[array.ndim - 3 + dim]
        if dim == axis:
            cuts.append(slice(1 + offset, extent - 1 + offset))
        else:
            cuts.append(slice(1, extent - 1))
    return array[tuple(cuts)]


def forward(array, axis):
    return window(array, axis, 1) - window(array, axis, 0)


def backward(array, axis):
    return window(array, axis, 0) - window(array, axis, -1)


def velocity_update(stress_pad, velocity, buoyancy):
    factor = STEP_TIME * buoyancy
    velocity_x = velocity[0] + factor * (forward(stress_pad[0], 0) + backward(stress_pad[3], 1) + backward(stress_pad[4], 2))
    velocity_y = velocity[1] + factor * (backward(stress_pad[3], 0) + forward(stress_pad[1], 1) + backward(stress_pad[5], 2))
    velocity_z = velocity[2] + factor * (backward(stress_pad[4], 0) + backward(stress_pad[5], 1) + forward(stress_pad[2], 2))
    return jnp.stack([velocity_x, velocity_y, velocity_z])


def stress_update(velocity_pad, stress, lame_lambda, shear_modulus):
    strain_x = backward(velocity_pad[0], 0)
    strain_y = backward(velocity_pad[1], 1)
    strain_z = backward(velocity_pad[2], 2)
    stiffness = lame_lambda + 2.0 * shear_modulus
    normal_x = stress[0] + STEP_TIME * (stiffness * strain_x + lame_lambda * (strain_y + strain_z))
    normal_y = stress[1] + STEP_TIME * (stiffness * strain_y + lame_lambda * (strain_x + strain_z))
    normal_z = stress[2] + STEP_TIME * (stiffness * strain_z + lame_lambda * (strain_x + strain_y))
    shear_xy = stress[3] + STEP_TIME * shear_modulus * (forward(velocity_pad[0], 1) + forward(velocity_pad[1], 0))
    shear_xz = stress[4] + STEP_TIME * shear_modulus * (forward(velocity_pad[0], 2) + forward(velocity_pad[2], 0))
    shear_yz = stress[5] + STEP_TIME * shear_modulus * (forward(velocity_pad[1], 2) + forward(velocity_pad[2], 1))
    return jnp.stack([normal_x, normal_y, normal_z, shear_xy, shear_xz, shear_yz])


def pad_cells(field):
    widths = [(0, 0)] * (field.ndim - 3) + [(1, 1)] * 3
    return jnp.pad(field, widths)


def build_frames(slip_rate, onsets):
    span = HOP * (STEPS - 1) + TAPS
    offsets = HOP * jnp.arange(STEPS, dtype=jnp.int32)[:, None] + jnp.arange(TAPS, dtype=jnp.int32)[None, :]

    def frames_of(row, start):
        return lax.dynamic_slice_in_dim(row, start.astype(jnp.int32), span)[offsets]

    return jax.vmap(frames_of)(slip_rate, onsets)


def reference(velocity, stress, buoyancy, lame_lambda, shear_modulus, slip_rate, taps, moment, cells, onsets):
    frames = build_frames(slip_rate, onsets)
    rates = jnp.einsum("fnk,k->nf", frames.astype(jnp.float32), taps.astype(jnp.float32))
    moment_rate = moment[:, None, :] * rates[None, :, :]

    def advance(step, carry):
        velocity_now, stress_now = carry
        velocity_now = velocity_update(pad_cells(stress_now), velocity_now, buoyancy)
        stress_now = stress_update(pad_cells(velocity_now), stress_now, lame_lambda, shear_modulus)
        source = lax.dynamic_index_in_dim(moment_rate, step, 1, keepdims=False)
        stress_now = stress_now.at[:, cells[0], cells[1], cells[2]].add(-STEP_TIME * source)
        return velocity_now, stress_now

    velocity_out, stress_out = lax.fori_loop(0, STEPS, advance, (velocity, stress))
    return velocity_out, stress_out
```

```python
import jax
import jax.numpy as jnp
from jax import lax
from jax.sharding import PartitionSpec as P

TAPS = 512
HOP = 64
STEPS = 16


STEP_TIME = 0.25
AXES = ("gx", "gy", "gz")


def to_next(block, axis):
    count = lax.axis_size(axis)
    return lax.ppermute(block, axis, [(i, i + 1) for i in range(count - 1)])


def to_prev(block, axis):
    count = lax.axis_size(axis)
    return lax.ppermute(block, axis, [(i + 1, i) for i in range(count - 1)])


def first(a, dim):
    return lax.slice_in_dim(a, 0, 1, axis=dim)


def last(a, dim):
    return lax.slice_in_dim(a, a.shape[dim] - 1, a.shape[dim], axis=dim)


def from_high(a, halo, dim):
    return jnp.concatenate([lax.slice_in_dim(a, 1, a.shape[dim], axis=dim), halo], axis=dim)


def from_low(a, halo, dim):
    return jnp.concatenate([halo, lax.slice_in_dim(a, 0, a.shape[dim] - 1, axis=dim)], axis=dim)


def velocity_update(stress, velocity, factor):
    sxx, syy, szz, sxy, sxz, syz = stress
    sxx_hx = to_prev(first(sxx, 0), "gx")
    low_x = to_next(jnp.stack([last(sxy, 0), last(sxz, 0)]), "gx")
    syy_hy = to_prev(first(syy, 1), "gy")
    low_y = to_next(jnp.stack([last(sxy, 1), last(syz, 1)]), "gy")
    szz_hz = to_prev(first(szz, 2), "gz")
    low_z = to_next(jnp.stack([last(sxz, 2), last(syz, 2)]), "gz")
    velocity_x = velocity[0] + factor * (
        (from_high(sxx, sxx_hx, 0) - sxx)
        + (sxy - from_low(sxy, low_y[0], 1))
        + (sxz - from_low(sxz, low_z[0], 2))
    )
    velocity_y = velocity[1] + factor * (
        (sxy - from_low(sxy, low_x[0], 0))
        + (from_high(syy, syy_hy, 1) - syy)
        + (syz - from_low(syz, low_z[1], 2))
    )
    velocity_z = velocity[2] + factor * (
        (sxz - from_low(sxz, low_x[1], 0))
        + (syz - from_low(syz, low_y[1], 1))
        + (from_high(szz, szz_hz, 2) - szz)
    )
    return (velocity_x, velocity_y, velocity_z)


def stress_update(velocity, stress, lame_lambda, shear_modulus, stiffness):
    vx, vy, vz = velocity
    vx_lx = to_next(last(vx, 0), "gx")
    high_x = to_prev(jnp.stack([first(vy, 0), first(vz, 0)]), "gx")
    vy_ly = to_next(last(vy, 1), "gy")
    high_y = to_prev(jnp.stack([first(vx, 1), first(vz, 1)]), "gy")
    vz_lz = to_next(last(vz, 2), "gz")
    high_z = to_prev(jnp.stack([first(vx, 2), first(vy, 2)]), "gz")
    strain_x = vx - from_low(vx, vx_lx, 0)
    strain_y = vy - from_low(vy, vy_ly, 1)
    strain_z = vz - from_low(vz, vz_lz, 2)
    normal_x = stress[0] + STEP_TIME * (stiffness * strain_x + lame_lambda * (strain_y + strain_z))
    normal_y = stress[1] + STEP_TIME * (stiffness * strain_y + lame_lambda * (strain_x + strain_z))
    normal_z = stress[2] + STEP_TIME * (stiffness * strain_z + lame_lambda * (strain_x + strain_y))
    shear_xy = stress[3] + STEP_TIME * shear_modulus * (
        (from_high(vx, high_y[0], 1) - vx) + (from_high(vy, high_x[0], 0) - vy)
    )
    shear_xz = stress[4] + STEP_TIME * shear_modulus * (
        (from_high(vx, high_z[0], 2) - vx) + (from_high(vz, high_x[1], 0) - vz)
    )
    shear_yz = stress[5] + STEP_TIME * shear_modulus * (
        (from_high(vy, high_z[1], 2) - vy) + (from_high(vz, high_y[1], 1) - vz)
    )
    return [normal_x, normal_y, normal_z, shear_xy, shear_xz, shear_yz]


def local_rates(slip_rate, taps, onsets):
    span = HOP * (STEPS - 1) + TAPS
    segments = jax.vmap(lambda row, start: lax.dynamic_slice_in_dim(row, start, span))(
        slip_rate, onsets
    )
    banded = jnp.stack(
        [jnp.pad(taps, (HOP * n, span - TAPS - HOP * n)) for n in range(STEPS)], axis=1
    )
    return jnp.dot(segments, banded, preferred_element_type=jnp.float32)


def on_device(
    velocity, stress, buoyancy, lame_lambda, shear_modulus, slip_rate, taps, moment, cells, onsets
):
    rates = local_rates(slip_rate, taps, onsets)
    rows = (rates[:, :, None] * moment.T[:, None, :]).reshape(rates.shape[0], -1)
    devices = lax.axis_size("gx") * lax.axis_size("gy") * lax.axis_size("gz")
    index = (lax.axis_index("gx") * lax.axis_size("gy") + lax.axis_index("gy")) * lax.axis_size(
        "gz"
    ) + lax.axis_index("gz")
    slots = jnp.zeros((rows.shape[0] * devices, rows.shape[1]), jnp.float32)
    slots = lax.dynamic_update_slice_in_dim(slots, rows, index * rows.shape[0], axis=0)
    gathered = lax.psum(slots, AXES)
    width_x, width_y, width_z = buoyancy.shape
    local_x = cells[0] - lax.axis_index("gx") * width_x
    local_y = cells[1] - lax.axis_index("gy") * width_y
    local_z = cells[2] - lax.axis_index("gz") * width_z
    inside = (
        (local_x >= 0)
        & (local_x < width_x)
        & (local_y >= 0)
        & (local_y < width_y)
        & (local_z >= 0)
        & (local_z < width_z)
    )
    cell_count = width_x * width_y * width_z
    flat = jnp.where(inside, (local_x * width_y + local_y) * width_z + local_z, cell_count)
    dense = jnp.zeros((cell_count + 1, gathered.shape[1]), jnp.float32)
    dense = dense.at[flat].add(-STEP_TIME * gathered)
    source = dense[:cell_count].reshape(width_x, width_y, width_z, STEPS, 6)
    source = jnp.transpose(source, (3, 4, 0, 1, 2))

    factor = STEP_TIME * buoyancy
    stiffness = lame_lambda + 2.0 * shear_modulus
    velocity_now = (velocity[0], velocity[1], velocity[2])
    stress_now = [stress[c] for c in range(6)]
    for step in range(STEPS):
        velocity_now = velocity_update(stress_now, velocity_now, factor)
        stress_now = stress_update(velocity_now, stress_now, lame_lambda, shear_modulus, stiffness)
        stress_now = [stress_now[c] + source[step, c] for c in range(6)]
    return (jnp.stack(velocity_now), jnp.stack(stress_now))


def solution(mesh):
    placed = (
        P(None, "gx", "gy", "gz"),
        P(None, "gx", "gy", "gz"),
        P("gx", "gy", "gz"),
        P("gx", "gy", "gz"),
        P("gx", "gy", "gz"),
        P(("gx", "gy", "gz"), None),
        P(),
        P(None, ("gx", "gy", "gz")),
        P(),
        P(("gx", "gy", "gz")),
    )
    return jax.shard_map(
        on_device,
        mesh=mesh,
        in_specs=placed,
        out_specs=(P(None, "gx", "gy", "gz"), P(None, "gx", "gy", "gz")),
        check_vma=False,
    )
```

```python
import jax
import jax.numpy as jnp
from jax import lax
from jax.sharding import PartitionSpec as P

TAPS = 512
HOP = 64
STEPS = 16


STEP_TIME = 0.25
AXES = ("gx", "gy", "gz")
BLOCK = 4


def to_next(block, axis):
    count = lax.axis_size(axis)
    return lax.ppermute(block, axis, [(i, i + 1) for i in range(count - 1)])


def to_prev(block, axis):
    count = lax.axis_size(axis)
    return lax.ppermute(block, axis, [(i + 1, i) for i in range(count - 1)])


def with_halo(block, width):
    for axis, dim in (("gx", 1), ("gy", 2), ("gz", 3)):
        extent = block.shape[dim]
        low = to_next(lax.slice_in_dim(block, extent - width, extent, axis=dim), axis)
        high = to_prev(lax.slice_in_dim(block, 0, width, axis=dim), axis)
        block = jnp.concatenate([low, block, high], axis=dim)
    return block


def up(a, dim):
    edge = jnp.zeros_like(lax.slice_in_dim(a, 0, 1, axis=dim))
    return jnp.concatenate([lax.slice_in_dim(a, 1, a.shape[dim], axis=dim), edge], axis=dim)


def down(a, dim):
    edge = jnp.zeros_like(lax.slice_in_dim(a, 0, 1, axis=dim))
    return jnp.concatenate([edge, lax.slice_in_dim(a, 0, a.shape[dim] - 1, axis=dim)], axis=dim)


def forward(a, dim):
    return up(a, dim) - a


def backward(a, dim):
    return a - down(a, dim)


def velocity_update(stress, velocity, factor):
    sxx, syy, szz, sxy, sxz, syz = stress
    velocity_x = velocity[0] + factor * (forward(sxx, 0) + backward(sxy, 1) + backward(sxz, 2))
    velocity_y = velocity[1] + factor * (backward(sxy, 0) + forward(syy, 1) + backward(syz, 2))
    velocity_z = velocity[2] + factor * (backward(sxz, 0) + backward(syz, 1) + forward(szz, 2))
    return [velocity_x, velocity_y, velocity_z]


def stress_update(velocity, stress, lame_lambda, shear_modulus, stiffness):
    vx, vy, vz = velocity
    strain_x = backward(vx, 0)
    strain_y = backward(vy, 1)
    strain_z = backward(vz, 2)
    normal_x = stress[0] + STEP_TIME * (stiffness * strain_x + lame_lambda * (strain_y + strain_z))
    normal_y = stress[1] + STEP_TIME * (stiffness * strain_y + lame_lambda * (strain_x + strain_z))
    normal_z = stress[2] + STEP_TIME * (stiffness * strain_z + lame_lambda * (strain_x + strain_y))
    shear_xy = stress[3] + STEP_TIME * shear_modulus * (forward(vx, 1) + forward(vy, 0))
    shear_xz = stress[4] + STEP_TIME * shear_modulus * (forward(vx, 2) + forward(vz, 0))
    shear_yz = stress[5] + STEP_TIME * shear_modulus * (forward(vy, 2) + forward(vz, 1))
    return [normal_x, normal_y, normal_z, shear_xy, shear_xz, shear_yz]


def local_rates(slip_rate, taps, onsets):
    span = HOP * (STEPS - 1) + TAPS
    segments = jax.vmap(lambda row, start: lax.dynamic_slice_in_dim(row, start, span))(
        slip_rate, onsets
    )
    banded = jnp.stack(
        [jnp.pad(taps, (HOP * n, span - TAPS - HOP * n)) for n in range(STEPS)], axis=1
    )
    return jnp.dot(segments, banded, preferred_element_type=jnp.float32)


def gather_rows(rows):
    for axis in ("gz", "gy", "gx"):
        count = lax.axis_size(axis)
        if count & (count - 1):
            rows = lax.all_gather(rows, axis, axis=0, tiled=True)
            continue
        index = lax.axis_index(axis)
        bit = 1
        while bit < count:
            other = lax.ppermute(rows, axis, [(i, i ^ bit) for i in range(count)])
            rows = jnp.where(
                (index & bit) == 0,
                jnp.concatenate([rows, other]),
                jnp.concatenate([other, rows]),
            )
            bit *= 2
    return rows


def on_device(
    velocity, stress, buoyancy, lame_lambda, shear_modulus, slip_rate, taps, moment, cells, onsets
):
    width_x, width_y, width_z = buoyancy.shape
    halo = min(BLOCK, width_x, width_y, width_z, STEPS)
    ext = (width_x + 2 * halo, width_y + 2 * halo, width_z + 2 * halo)
    origin = (
        lax.axis_index("gx") * width_x - halo,
        lax.axis_index("gy") * width_y - halo,
        lax.axis_index("gz") * width_z - halo,
    )
    total = (
        width_x * lax.axis_size("gx"),
        width_y * lax.axis_size("gy"),
        width_z * lax.axis_size("gz"),
    )

    rates = local_rates(slip_rate, taps, onsets)
    rows = (rates[:, :, None] * moment.T[:, None, :]).reshape(rates.shape[0], -1)
    gathered = gather_rows(rows)
    row_low = total[1] // 2 - 1
    row = cells[1] - row_low
    local_x = cells[0] - origin[0]
    local_z = cells[2] - origin[2]
    inside = (
        (row >= 0)
        & (row < 2)
        & (local_x >= 0)
        & (local_x < ext[0])
        & (local_z >= 0)
        & (local_z < ext[2])
    )
    cell_count = 2 * ext[0] * ext[2]
    flat = jnp.where(inside, (row * ext[0] + local_x) * ext[2] + local_z, cell_count)
    strip = jnp.zeros((gathered.shape[1], cell_count), jnp.float32)
    strip = strip.at[:, flat].add(-STEP_TIME * gathered.T, mode="drop")
    strip = strip.reshape(gathered.shape[1], 2, ext[0], 1, ext[2])
    across = lax.broadcasted_iota(jnp.int32, ext, 1) + origin[1]
    on_low = across == row_low
    on_high = across == row_low + 1

    keep = None
    for d in range(3):
        where = origin[d] + lax.broadcasted_iota(jnp.int32, ext, d)
        inside_d = (where >= 0) & (where < total[d])
        keep = inside_d if keep is None else keep & inside_d

    media = with_halo(jnp.stack([buoyancy, lame_lambda, shear_modulus]), halo)
    factor = STEP_TIME * media[0]
    lame_ext = media[1]
    shear_ext = media[2]
    stiffness = lame_ext + 2.0 * shear_ext

    def run_block(fields, rows_of_block, count):
        block = with_halo(fields, halo)
        velocity_now = [block[c] for c in range(3)]
        stress_now = [block[3 + c] for c in range(6)]
        for step in range(count):
            velocity_now = velocity_update(stress_now, velocity_now, factor)
            velocity_now = [jnp.where(keep, v, 0.0) for v in velocity_now]
            stress_now = stress_update(velocity_now, stress_now, lame_ext, shear_ext, stiffness)
            stress_now = [
                jnp.where(
                    keep,
                    stress_now[c]
                    + (
                        jnp.where(on_low, rows_of_block[step * 6 + c, 0], 0.0)
                        + jnp.where(on_high, rows_of_block[step * 6 + c, 1], 0.0)
                    ),
                    0.0,
                )
                for c in range(6)
            ]
        block = jnp.stack(velocity_now + stress_now)
        return block[:, halo : halo + width_x, halo : halo + width_y, halo : halo + width_z]

    blocks = STEPS // halo
    rest = STEPS - blocks * halo
    per_block = strip[: blocks * halo * 6].reshape((blocks, halo * 6) + strip.shape[1:])

    def body(index, fields):
        rows_of_block = lax.dynamic_index_in_dim(per_block, index, 0, keepdims=False)
        return run_block(fields, rows_of_block, halo)

    fields = lax.fori_loop(0, blocks, body, jnp.concatenate([velocity, stress]))
    if rest:
        fields = run_block(fields, strip[blocks * halo * 6 :], rest)
    return (fields[:3], fields[3:])


def solution(mesh):
    placed = (
        P(None, "gx", "gy", "gz"),
        P(None, "gx", "gy", "gz"),
        P("gx", "gy", "gz"),
        P("gx", "gy", "gz"),
        P("gx", "gy", "gz"),
        P(("gx", "gy", "gz"), None),
        P(),
        P(None, ("gx", "gy", "gz")),
        P(),
        P(("gx", "gy", "gz")),
    )
    return jax.shard_map(
        on_device,
        mesh=mesh,
        in_specs=placed,
        out_specs=(P(None, "gx", "gy", "gz"), P(None, "gx", "gy", "gz")),
        check_vma=False,
    )
```

```python
import jax
import jax.numpy as jnp
from jax import lax
from jax.sharding import PartitionSpec as P

TAPS = 512
HOP = 64
STEPS = 16


STEP_TIME = 0.25
AXES = ("gx", "gy", "gz")
BLOCK = 4


def to_next(block, axis):
    count = lax.axis_size(axis)
    return lax.ppermute(block, axis, [(i, i + 1) for i in range(count - 1)])


def to_prev(block, axis):
    count = lax.axis_size(axis)
    return lax.ppermute(block, axis, [(i + 1, i) for i in range(count - 1)])


def with_halo(block, width):
    for axis, dim in (("gx", 1), ("gy", 2), ("gz", 3)):
        extent = block.shape[dim]
        low = to_next(lax.slice_in_dim(block, extent - width, extent, axis=dim), axis)
        high = to_prev(lax.slice_in_dim(block, 0, width, axis=dim), axis)
        block = jnp.concatenate([low, block, high], axis=dim)
    return block


def up(a, dim):
    edge = jnp.zeros_like(lax.slice_in_dim(a, 0, 1, axis=dim))
    return jnp.concatenate([lax.slice_in_dim(a, 1, a.shape[dim], axis=dim), edge], axis=dim)


def down(a, dim):
    edge = jnp.zeros_like(lax.slice_in_dim(a, 0, 1, axis=dim))
    return jnp.concatenate([edge, lax.slice_in_dim(a, 0, a.shape[dim] - 1, axis=dim)], axis=dim)


def forward(a, dim):
    return up(a, dim) - a


def backward(a, dim):
    return a - down(a, dim)


def velocity_update(stress, velocity, factor):
    sxx, syy, szz, sxy, sxz, syz = stress
    velocity_x = velocity[0] + factor * (forward(sxx, 0) + backward(sxy, 1) + backward(sxz, 2))
    velocity_y = velocity[1] + factor * (backward(sxy, 0) + forward(syy, 1) + backward(syz, 2))
    velocity_z = velocity[2] + factor * (backward(sxz, 0) + backward(syz, 1) + forward(szz, 2))
    return [velocity_x, velocity_y, velocity_z]


def stress_update(velocity, stress, lame_lambda, shear_modulus, stiffness):
    vx, vy, vz = velocity
    strain_x = backward(vx, 0)
    strain_y = backward(vy, 1)
    strain_z = backward(vz, 2)
    normal_x = stress[0] + STEP_TIME * (stiffness * strain_x + lame_lambda * (strain_y + strain_z))
    normal_y = stress[1] + STEP_TIME * (stiffness * strain_y + lame_lambda * (strain_x + strain_z))
    normal_z = stress[2] + STEP_TIME * (stiffness * strain_z + lame_lambda * (strain_x + strain_y))
    shear_xy = stress[3] + STEP_TIME * shear_modulus * (forward(vx, 1) + forward(vy, 0))
    shear_xz = stress[4] + STEP_TIME * shear_modulus * (forward(vx, 2) + forward(vz, 0))
    shear_yz = stress[5] + STEP_TIME * shear_modulus * (forward(vy, 2) + forward(vz, 1))
    return [normal_x, normal_y, normal_z, shear_xy, shear_xz, shear_yz]


def local_rates(slip_rate, taps, onsets):
    span = HOP * (STEPS - 1) + TAPS
    segments = jax.vmap(lambda row, start: lax.dynamic_slice_in_dim(row, start, span))(
        slip_rate, onsets
    )
    banded = jnp.stack(
        [jnp.pad(taps, (HOP * n, span - TAPS - HOP * n)) for n in range(STEPS)], axis=1
    )
    return jnp.dot(segments, banded, preferred_element_type=jnp.float32)


def gather_rows(rows):
    for axis in ("gz", "gy", "gx"):
        count = lax.axis_size(axis)
        if count & (count - 1):
            rows = lax.all_gather(rows, axis, axis=0, tiled=True)
            continue
        index = lax.axis_index(axis)
        bit = 1
        while bit < count:
            other = lax.ppermute(rows, axis, [(i, i ^ bit) for i in range(count)])
            rows = jnp.where(
                (index & bit) == 0,
                jnp.concatenate([rows, other]),
                jnp.concatenate([other, rows]),
            )
            bit *= 2
    return rows


def on_device(
    velocity, stress, buoyancy, lame_lambda, shear_modulus, slip_rate, taps, moment, cells, onsets
):
    width_x, width_y, width_z = buoyancy.shape
    halo = min(BLOCK, width_x, width_y, width_z, STEPS)
    ext = (width_x + 2 * halo, width_y + 2 * halo, width_z + 2 * halo)
    origin = (
        lax.axis_index("gx") * width_x - halo,
        lax.axis_index("gy") * width_y - halo,
        lax.axis_index("gz") * width_z - halo,
    )
    total = (
        width_x * lax.axis_size("gx"),
        width_y * lax.axis_size("gy"),
        width_z * lax.axis_size("gz"),
    )

    rates = local_rates(slip_rate, taps, onsets)
    rows = (rates[:, :, None] * moment.T[:, None, :]).reshape(rates.shape[0], -1)
    gathered = gather_rows(rows)
    row_low = total[1] // 2 - 1
    row = cells[1] - row_low
    local_x = cells[0] - origin[0]
    local_z = cells[2] - origin[2]
    inside = (
        (row >= 0)
        & (row < 2)
        & (local_x >= 0)
        & (local_x < ext[0])
        & (local_z >= 0)
        & (local_z < ext[2])
    )
    cell_count = 2 * ext[0] * ext[2]
    flat = jnp.where(inside, (row * ext[0] + local_x) * ext[2] + local_z, cell_count)
    strip = jnp.zeros((gathered.shape[1], cell_count), jnp.float32)
    strip = strip.at[:, flat].add(-STEP_TIME * gathered.T, mode="drop")
    strip = strip.reshape(gathered.shape[1], 2, ext[0], ext[2])
    across = lax.broadcasted_iota(jnp.int32, ext, 1) + origin[1]
    on_low = across == row_low
    on_high = across == row_low + 1

    keep = None
    for d in range(3):
        where = origin[d] + lax.broadcasted_iota(jnp.int32, ext, d)
        inside_d = (where >= 0) & (where < total[d])
        keep = inside_d if keep is None else keep & inside_d

    media = with_halo(jnp.stack([buoyancy, lame_lambda, shear_modulus]), halo)
    factor = STEP_TIME * media[0]
    lame_ext = media[1]
    shear_ext = media[2]
    stiffness = lame_ext + 2.0 * shear_ext

    def run_block(fields, rows_of_block, count):
        block = with_halo(fields, halo)
        velocity_now = [block[c] for c in range(3)]
        stress_now = [block[3 + c] for c in range(6)]
        added = jnp.where(on_low, rows_of_block[:, 0][:, :, None, :], 0.0) + jnp.where(
            on_high, rows_of_block[:, 1][:, :, None, :], 0.0
        )
        for step in range(count):
            velocity_now = velocity_update(stress_now, velocity_now, factor)
            velocity_now = [jnp.where(keep, v, 0.0) for v in velocity_now]
            stress_now = stress_update(velocity_now, stress_now, lame_ext, shear_ext, stiffness)
            stress_now = [
                jnp.where(keep, stress_now[c] + added[step * 6 + c], 0.0) for c in range(6)
            ]
        block = jnp.stack(velocity_now + stress_now)
        return block[:, halo : halo + width_x, halo : halo + width_y, halo : halo + width_z]

    blocks = STEPS // halo
    rest = STEPS - blocks * halo
    per_block = strip[: blocks * halo * 6].reshape((blocks, halo * 6) + strip.shape[1:])

    def body(index, fields):
        rows_of_block = lax.dynamic_index_in_dim(per_block, index, 0, keepdims=False)
        return run_block(fields, rows_of_block, halo)

    fields = jnp.concatenate([velocity, stress])
    if blocks:
        fields = run_block(fields, per_block[0], halo)
    fields = lax.fori_loop(1, blocks, body, fields)
    if rest:
        fields = run_block(fields, strip[blocks * halo * 6 :], rest)
    return (fields[:3], fields[3:])


def solution(mesh):
    placed = (
        P(None, "gx", "gy", "gz"),
        P(None, "gx", "gy", "gz"),
        P("gx", "gy", "gz"),
        P("gx", "gy", "gz"),
        P("gx", "gy", "gz"),
        P(("gx", "gy", "gz"), None),
        P(),
        P(None, ("gx", "gy", "gz")),
        P(),
        P(("gx", "gy", "gz")),
    )
    return jax.shard_map(
        on_device,
        mesh=mesh,
        in_specs=placed,
        out_specs=(P(None, "gx", "gy", "gz"), P(None, "gx", "gy", "gz")),
        check_vma=False,
    )
```

```python
import jax
import jax.numpy as jnp
from jax import lax
from jax.sharding import PartitionSpec as P

TAPS = 512
HOP = 64
STEPS = 16


STEP_TIME = 0.25
AXES = ("gx", "gy", "gz")
BLOCK = 4


def to_next(block, axis):
    count = lax.axis_size(axis)
    return lax.ppermute(block, axis, [(i, i + 1) for i in range(count - 1)])


def to_prev(block, axis):
    count = lax.axis_size(axis)
    return lax.ppermute(block, axis, [(i + 1, i) for i in range(count - 1)])


def with_halo(block, width):
    for axis, dim in (("gx", 1), ("gy", 2), ("gz", 3)):
        extent = block.shape[dim]
        low = to_next(lax.slice_in_dim(block, extent - width, extent, axis=dim), axis)
        high = to_prev(lax.slice_in_dim(block, 0, width, axis=dim), axis)
        block = jnp.concatenate([low, block, high], axis=dim)
    return block


def up(a, dim):
    edge = jnp.zeros_like(lax.slice_in_dim(a, 0, 1, axis=dim))
    return jnp.concatenate([lax.slice_in_dim(a, 1, a.shape[dim], axis=dim), edge], axis=dim)


def down(a, dim):
    edge = jnp.zeros_like(lax.slice_in_dim(a, 0, 1, axis=dim))
    return jnp.concatenate([edge, lax.slice_in_dim(a, 0, a.shape[dim] - 1, axis=dim)], axis=dim)


def forward(a, dim):
    return up(a, dim) - a


def backward(a, dim):
    return a - down(a, dim)


def velocity_update(stress, velocity, factor):
    sxx, syy, szz, sxy, sxz, syz = stress
    velocity_x = velocity[0] + factor * (forward(sxx, 0) + backward(sxy, 1) + backward(sxz, 2))
    velocity_y = velocity[1] + factor * (backward(sxy, 0) + forward(syy, 1) + backward(syz, 2))
    velocity_z = velocity[2] + factor * (backward(sxz, 0) + backward(syz, 1) + forward(szz, 2))
    return [velocity_x, velocity_y, velocity_z]


def stress_update(velocity, stress, lame_lambda, shear_modulus, stiffness):
    vx, vy, vz = velocity
    strain_x = backward(vx, 0)
    strain_y = backward(vy, 1)
    strain_z = backward(vz, 2)
    normal_x = stress[0] + STEP_TIME * (stiffness * strain_x + lame_lambda * (strain_y + strain_z))
    normal_y = stress[1] + STEP_TIME * (stiffness * strain_y + lame_lambda * (strain_x + strain_z))
    normal_z = stress[2] + STEP_TIME * (stiffness * strain_z + lame_lambda * (strain_x + strain_y))
    shear_xy = stress[3] + STEP_TIME * shear_modulus * (forward(vx, 1) + forward(vy, 0))
    shear_xz = stress[4] + STEP_TIME * shear_modulus * (forward(vx, 2) + forward(vz, 0))
    shear_yz = stress[5] + STEP_TIME * shear_modulus * (forward(vy, 2) + forward(vz, 1))
    return [normal_x, normal_y, normal_z, shear_xy, shear_xz, shear_yz]


def local_rates(slip_rate, taps, onsets):
    span = HOP * (STEPS - 1) + TAPS
    segments = jnp.concatenate(
        [
            lax.dynamic_slice(slip_rate, (f, onsets[f]), (1, span))
            for f in range(slip_rate.shape[0])
        ]
    )
    banded = jnp.stack(
        [jnp.pad(taps, (HOP * n, span - TAPS - HOP * n)) for n in range(STEPS)], axis=1
    )
    return jnp.dot(segments, banded, preferred_element_type=jnp.float32)


def gather_rows(rows):
    for axis in ("gz", "gy", "gx"):
        count = lax.axis_size(axis)
        if count & (count - 1):
            rows = lax.all_gather(rows, axis, axis=0, tiled=True)
            continue
        index = lax.axis_index(axis)
        stride = 1
        while stride < count:
            radix = 4 if count % (stride * 4) == 0 else 2
            place = (index // stride) % radix
            pieces = [rows]
            for shift in range(1, radix):
                pairs = []
                for source in range(count):
                    at = (source // stride) % radix
                    pairs.append((source, source + ((at - shift) % radix - at) * stride))
                pieces.append(lax.ppermute(rows, axis, pairs))
            order = (jnp.arange(radix) - place) % radix
            rows = jnp.stack(pieces)[order].reshape(-1, rows.shape[-1])
            stride *= radix
    return rows


def on_device(
    velocity, stress, buoyancy, lame_lambda, shear_modulus, slip_rate, taps, moment, cells, onsets
):
    width_x, width_y, width_z = buoyancy.shape
    halo = min(BLOCK, width_x, width_y, width_z, STEPS)
    ext = (width_x + 2 * halo, width_y + 2 * halo, width_z + 2 * halo)
    origin = (
        lax.axis_index("gx") * width_x - halo,
        lax.axis_index("gy") * width_y - halo,
        lax.axis_index("gz") * width_z - halo,
    )
    total = (
        width_x * lax.axis_size("gx"),
        width_y * lax.axis_size("gy"),
        width_z * lax.axis_size("gz"),
    )

    rates = local_rates(slip_rate, taps, onsets)
    rows = (rates[:, :, None] * moment.T[:, None, :]).reshape(rates.shape[0], -1)
    gathered = gather_rows(rows)
    row_low = total[1] // 2 - 1
    row = cells[1] - row_low
    local_x = cells[0] - origin[0]
    local_z = cells[2] - origin[2]
    inside = (
        (row >= 0)
        & (row < 2)
        & (local_x >= 0)
        & (local_x < ext[0])
        & (local_z >= 0)
        & (local_z < ext[2])
    )
    cell_count = 2 * ext[0] * ext[2]
    flat = jnp.where(inside, (row * ext[0] + local_x) * ext[2] + local_z, cell_count)
    strip = jnp.zeros((gathered.shape[1], cell_count), jnp.float32)
    strip = strip.at[:, flat].add(-STEP_TIME * gathered.T, mode="drop")
    strip = strip.reshape(gathered.shape[1], 2, ext[0], ext[2])
    across = lax.broadcasted_iota(jnp.int32, ext, 1) + origin[1]
    on_low = across == row_low
    on_high = across == row_low + 1

    keep = None
    for d in range(3):
        where = origin[d] + lax.broadcasted_iota(jnp.int32, ext, d)
        inside_d = (where >= 0) & (where < total[d])
        keep = inside_d if keep is None else keep & inside_d

    media = with_halo(jnp.stack([buoyancy, lame_lambda, shear_modulus]), halo)
    factor = STEP_TIME * media[0]
    lame_ext = media[1]
    shear_ext = media[2]
    stiffness = lame_ext + 2.0 * shear_ext

    def run_block(fields, rows_of_block, count):
        block = with_halo(fields, halo)
        velocity_now = [block[c] for c in range(3)]
        stress_now = [block[3 + c] for c in range(6)]
        added = jnp.where(on_low, rows_of_block[:, 0][:, :, None, :], 0.0) + jnp.where(
            on_high, rows_of_block[:, 1][:, :, None, :], 0.0
        )
        for step in range(count):
            velocity_now = velocity_update(stress_now, velocity_now, factor)
            velocity_now = [jnp.where(keep, v, 0.0) for v in velocity_now]
            stress_now = stress_update(velocity_now, stress_now, lame_ext, shear_ext, stiffness)
            stress_now = [
                jnp.where(keep, stress_now[c] + added[step * 6 + c], 0.0) for c in range(6)
            ]
        block = jnp.stack(velocity_now + stress_now)
        return block[:, halo : halo + width_x, halo : halo + width_y, halo : halo + width_z]

    blocks = STEPS // halo
    rest = STEPS - blocks * halo
    per_block = strip[: blocks * halo * 6].reshape((blocks, halo * 6) + strip.shape[1:])

    def body(index, fields):
        rows_of_block = lax.dynamic_index_in_dim(per_block, index, 0, keepdims=False)
        return run_block(fields, rows_of_block, halo)

    fields = jnp.concatenate([velocity, stress])
    if blocks:
        fields = run_block(fields, per_block[0], halo)
    fields = lax.fori_loop(1, blocks, body, fields)
    if rest:
        fields = run_block(fields, strip[blocks * halo * 6 :], rest)
    return (fields[:3], fields[3:])


def solution(mesh):
    placed = (
        P(None, "gx", "gy", "gz"),
        P(None, "gx", "gy", "gz"),
        P("gx", "gy", "gz"),
        P("gx", "gy", "gz"),
        P("gx", "gy", "gz"),
        P(("gx", "gy", "gz"), None),
        P(),
        P(None, ("gx", "gy", "gz")),
        P(),
        P(("gx", "gy", "gz")),
    )
    return jax.shard_map(
        on_device,
        mesh=mesh,
        in_specs=placed,
        out_specs=(P(None, "gx", "gy", "gz"), P(None, "gx", "gy", "gz")),
        check_vma=False,
    )
```

```python
import jax
import jax.numpy as jnp
from jax import lax
from jax.sharding import PartitionSpec as P

TAPS = 512
HOP = 64
STEPS = 16


STEP_TIME = 0.25
AXES = ("gx", "gy", "gz")
BLOCK = 4


def to_next(block, axis):
    count = lax.axis_size(axis)
    return lax.ppermute(block, axis, [(i, i + 1) for i in range(count - 1)])


def to_prev(block, axis):
    count = lax.axis_size(axis)
    return lax.ppermute(block, axis, [(i + 1, i) for i in range(count - 1)])


def with_halo(block, width):
    for axis, dim in (("gx", 1), ("gy", 2), ("gz", 3)):
        extent = block.shape[dim]
        low = to_next(lax.slice_in_dim(block, extent - width, extent, axis=dim), axis)
        high = to_prev(lax.slice_in_dim(block, 0, width, axis=dim), axis)
        block = jnp.concatenate([low, block, high], axis=dim)
    return block


def up(a, dim):
    edge = jnp.zeros_like(lax.slice_in_dim(a, 0, 1, axis=dim))
    return jnp.concatenate([lax.slice_in_dim(a, 1, a.shape[dim], axis=dim), edge], axis=dim)


def down(a, dim):
    edge = jnp.zeros_like(lax.slice_in_dim(a, 0, 1, axis=dim))
    return jnp.concatenate([edge, lax.slice_in_dim(a, 0, a.shape[dim] - 1, axis=dim)], axis=dim)


def forward(a, dim):
    return up(a, dim) - a


def backward(a, dim):
    return a - down(a, dim)


def velocity_update(stress, velocity, factor):
    sxx, syy, szz, sxy, sxz, syz = stress
    velocity_x = velocity[0] + factor * (forward(sxx, 0) + backward(sxy, 1) + backward(sxz, 2))
    velocity_y = velocity[1] + factor * (backward(sxy, 0) + forward(syy, 1) + backward(syz, 2))
    velocity_z = velocity[2] + factor * (backward(sxz, 0) + backward(syz, 1) + forward(szz, 2))
    return [velocity_x, velocity_y, velocity_z]


def stress_update(velocity, stress, lame_lambda, shear_modulus, stiffness):
    vx, vy, vz = velocity
    strain_x = backward(vx, 0)
    strain_y = backward(vy, 1)
    strain_z = backward(vz, 2)
    normal_x = stress[0] + STEP_TIME * (stiffness * strain_x + lame_lambda * (strain_y + strain_z))
    normal_y = stress[1] + STEP_TIME * (stiffness * strain_y + lame_lambda * (strain_x + strain_z))
    normal_z = stress[2] + STEP_TIME * (stiffness * strain_z + lame_lambda * (strain_x + strain_y))
    shear_xy = stress[3] + STEP_TIME * shear_modulus * (forward(vx, 1) + forward(vy, 0))
    shear_xz = stress[4] + STEP_TIME * shear_modulus * (forward(vx, 2) + forward(vz, 0))
    shear_yz = stress[5] + STEP_TIME * shear_modulus * (forward(vy, 2) + forward(vz, 1))
    return [normal_x, normal_y, normal_z, shear_xy, shear_xz, shear_yz]


def local_rates(slip_rate, taps, onsets):
    span = HOP * (STEPS - 1) + TAPS
    segments = jnp.concatenate(
        [
            lax.dynamic_slice(slip_rate, (f, onsets[f]), (1, span))
            for f in range(slip_rate.shape[0])
        ]
    )
    banded = jnp.stack(
        [jnp.pad(taps, (HOP * n, span - TAPS - HOP * n)) for n in range(STEPS)], axis=1
    )
    return jnp.dot(segments, banded, preferred_element_type=jnp.float32)


def gather_rows(rows):
    for axis in ("gz", "gy", "gx"):
        count = lax.axis_size(axis)
        if count & (count - 1):
            rows = lax.all_gather(rows, axis, axis=0, tiled=True)
            continue
        index = lax.axis_index(axis)
        stride = 1
        while stride < count:
            radix = 4 if count % (stride * 4) == 0 else 2
            place = (index // stride) % radix
            pieces = [rows]
            for shift in range(1, radix):
                pairs = []
                for source in range(count):
                    at = (source // stride) % radix
                    pairs.append((source, source + ((at - shift) % radix - at) * stride))
                pieces.append(lax.ppermute(rows, axis, pairs))
            order = (jnp.arange(radix) - place) % radix
            rows = jnp.stack(pieces)[order].reshape(-1, rows.shape[-1])
            stride *= radix
    return rows


def on_device(
    velocity, stress, buoyancy, lame_lambda, shear_modulus, slip_rate, taps, moment, cells, onsets
):
    width_x, width_y, width_z = buoyancy.shape
    halo = min(BLOCK, width_x, width_y, width_z, STEPS)
    ext = (width_x + 2 * halo, width_y + 2 * halo, width_z + 2 * halo)
    origin = (
        lax.axis_index("gx") * width_x - halo,
        lax.axis_index("gy") * width_y - halo,
        lax.axis_index("gz") * width_z - halo,
    )
    total = (
        width_x * lax.axis_size("gx"),
        width_y * lax.axis_size("gy"),
        width_z * lax.axis_size("gz"),
    )

    rates = local_rates(slip_rate, taps, onsets)
    local_count = rates.shape[0]
    packed = jnp.concatenate([rates.reshape(-1), moment.T.reshape(-1)])
    lanes = -(-packed.shape[0] // 128) * 128
    packed = jnp.pad(packed, (0, lanes - packed.shape[0])).reshape(lanes // 128, 128)
    packed = gather_rows(packed).reshape(-1, lanes)
    rates_all = packed[:, : local_count * STEPS].reshape(-1, STEPS)
    moment_all = packed[:, local_count * STEPS : local_count * (STEPS + 6)].reshape(-1, 6)
    gathered = (rates_all[:, :, None] * moment_all[:, None, :]).reshape(rates_all.shape[0], -1)
    row_low = total[1] // 2 - 1
    row = cells[1] - row_low
    local_x = cells[0] - origin[0]
    local_z = cells[2] - origin[2]
    inside = (
        (row >= 0)
        & (row < 2)
        & (local_x >= 0)
        & (local_x < ext[0])
        & (local_z >= 0)
        & (local_z < ext[2])
    )
    row = jnp.where(inside, row, 2)
    local_x = jnp.where(inside, local_x, ext[0])
    local_z = jnp.where(inside, local_z, ext[2])
    strip = jnp.zeros((gathered.shape[1], 2, ext[0], ext[2]), jnp.float32)
    strip = strip.at[:, row, local_x, local_z].add(-STEP_TIME * gathered.T, mode="drop")
    across = lax.broadcasted_iota(jnp.int32, ext, 1) + origin[1]
    on_low = across == row_low
    on_high = across == row_low + 1

    keep = None
    for d in range(3):
        where = origin[d] + lax.broadcasted_iota(jnp.int32, ext, d)
        inside_d = (where >= 0) & (where < total[d])
        keep = inside_d if keep is None else keep & inside_d

    media = with_halo(jnp.stack([buoyancy, lame_lambda, shear_modulus]), halo)
    factor = STEP_TIME * media[0]
    lame_ext = media[1]
    shear_ext = media[2]
    stiffness = lame_ext + 2.0 * shear_ext

    def run_block(fields, rows_of_block, count):
        block = with_halo(fields, halo)
        velocity_now = [block[c] for c in range(3)]
        stress_now = [block[3 + c] for c in range(6)]
        added = jnp.where(on_low, rows_of_block[:, 0][:, :, None, :], 0.0) + jnp.where(
            on_high, rows_of_block[:, 1][:, :, None, :], 0.0
        )
        for step in range(count):
            velocity_now = velocity_update(stress_now, velocity_now, factor)
            velocity_now = [jnp.where(keep, v, 0.0) for v in velocity_now]
            stress_now = stress_update(velocity_now, stress_now, lame_ext, shear_ext, stiffness)
            stress_now = [
                jnp.where(keep, stress_now[c] + added[step * 6 + c], 0.0) for c in range(6)
            ]
        block = jnp.stack(velocity_now + stress_now)
        return block[:, halo : halo + width_x, halo : halo + width_y, halo : halo + width_z]

    blocks = STEPS // halo
    rest = STEPS - blocks * halo
    per_block = strip[: blocks * halo * 6].reshape((blocks, halo * 6) + strip.shape[1:])

    def body(index, fields):
        rows_of_block = lax.dynamic_index_in_dim(per_block, index, 0, keepdims=False)
        return run_block(fields, rows_of_block, halo)

    fields = jnp.concatenate([velocity, stress])
    if blocks:
        fields = run_block(fields, per_block[0], halo)
    fields = lax.fori_loop(1, blocks, body, fields)
    if rest:
        fields = run_block(fields, strip[blocks * halo * 6 :], rest)
    return (fields[:3], fields[3:])


def solution(mesh):
    placed = (
        P(None, "gx", "gy", "gz"),
        P(None, "gx", "gy", "gz"),
        P("gx", "gy", "gz"),
        P("gx", "gy", "gz"),
        P("gx", "gy", "gz"),
        P(("gx", "gy", "gz"), None),
        P(),
        P(None, ("gx", "gy", "gz")),
        P(),
        P(("gx", "gy", "gz")),
    )
    return jax.shard_map(
        on_device,
        mesh=mesh,
        in_specs=placed,
        out_specs=(P(None, "gx", "gy", "gz"), P(None, "gx", "gy", "gz")),
        check_vma=False,
    )
```

```python
import jax
import jax.numpy as jnp
from jax import lax
from jax.sharding import PartitionSpec as P

TAPS = 512
HOP = 64
STEPS = 16


STEP_TIME = 0.25
AXES = ("gx", "gy", "gz")
BLOCK = 4


def to_next(block, axis):
    count = lax.axis_size(axis)
    return lax.ppermute(block, axis, [(i, i + 1) for i in range(count - 1)])


def to_prev(block, axis):
    count = lax.axis_size(axis)
    return lax.ppermute(block, axis, [(i + 1, i) for i in range(count - 1)])


def with_halo(block, width):
    for axis, dim in (("gx", 1), ("gy", 2), ("gz", 3)):
        extent = block.shape[dim]
        low = to_next(lax.slice_in_dim(block, extent - width, extent, axis=dim), axis)
        high = to_prev(lax.slice_in_dim(block, 0, width, axis=dim), axis)
        block = jnp.concatenate([low, block, high], axis=dim)
    return block


def up(a, dim):
    edge = jnp.zeros_like(lax.slice_in_dim(a, 0, 1, axis=dim))
    return jnp.concatenate([lax.slice_in_dim(a, 1, a.shape[dim], axis=dim), edge], axis=dim)


def down(a, dim):
    edge = jnp.zeros_like(lax.slice_in_dim(a, 0, 1, axis=dim))
    return jnp.concatenate([edge, lax.slice_in_dim(a, 0, a.shape[dim] - 1, axis=dim)], axis=dim)


def forward(a, dim):
    return up(a, dim) - a


def backward(a, dim):
    return a - down(a, dim)


def velocity_update(stress, velocity, factor):
    sxx, syy, szz, sxy, sxz, syz = stress
    velocity_x = velocity[0] + factor * (forward(sxx, 0) + backward(sxy, 1) + backward(sxz, 2))
    velocity_y = velocity[1] + factor * (backward(sxy, 0) + forward(syy, 1) + backward(syz, 2))
    velocity_z = velocity[2] + factor * (backward(sxz, 0) + backward(syz, 1) + forward(szz, 2))
    return [velocity_x, velocity_y, velocity_z]


def stress_update(velocity, stress, lame_lambda, shear_modulus, stiffness):
    vx, vy, vz = velocity
    strain_x = backward(vx, 0)
    strain_y = backward(vy, 1)
    strain_z = backward(vz, 2)
    normal_x = stress[0] + STEP_TIME * (stiffness * strain_x + lame_lambda * (strain_y + strain_z))
    normal_y = stress[1] + STEP_TIME * (stiffness * strain_y + lame_lambda * (strain_x + strain_z))
    normal_z = stress[2] + STEP_TIME * (stiffness * strain_z + lame_lambda * (strain_x + strain_y))
    shear_xy = stress[3] + STEP_TIME * shear_modulus * (forward(vx, 1) + forward(vy, 0))
    shear_xz = stress[4] + STEP_TIME * shear_modulus * (forward(vx, 2) + forward(vz, 0))
    shear_yz = stress[5] + STEP_TIME * shear_modulus * (forward(vy, 2) + forward(vz, 1))
    return [normal_x, normal_y, normal_z, shear_xy, shear_xz, shear_yz]


def local_rates(slip_rate, taps, onsets):
    span = HOP * (STEPS - 1) + TAPS
    segments = jnp.concatenate(
        [
            lax.dynamic_slice(slip_rate, (f, onsets[f]), (1, span))
            for f in range(slip_rate.shape[0])
        ]
    )
    banded = jnp.stack(
        [jnp.pad(taps, (HOP * n, span - TAPS - HOP * n)) for n in range(STEPS)], axis=1
    )
    return jnp.dot(segments, banded, preferred_element_type=jnp.float32)


def gather_rows(rows):
    for axis in ("gz", "gy", "gx"):
        count = lax.axis_size(axis)
        if count & (count - 1):
            rows = lax.all_gather(rows, axis, axis=0, tiled=True)
            continue
        index = lax.axis_index(axis)
        stride = 1
        while stride < count:
            radix = 4 if count % (stride * 4) == 0 else 2
            place = (index // stride) % radix
            pieces = [rows]
            for shift in range(1, radix):
                pairs = []
                for source in range(count):
                    at = (source // stride) % radix
                    pairs.append((source, source + ((at - shift) % radix - at) * stride))
                pieces.append(lax.ppermute(rows, axis, pairs))
            order = (jnp.arange(radix) - place) % radix
            rows = jnp.stack(pieces)[order].reshape(-1, rows.shape[-1])
            stride *= radix
    return rows


def on_device(
    velocity, stress, buoyancy, lame_lambda, shear_modulus, slip_rate, taps, moment, cells, onsets
):
    width_x, width_y, width_z = buoyancy.shape
    halo = min(BLOCK, width_x, width_y, width_z, STEPS)
    ext = (width_x + 2 * halo, width_y + 2 * halo, width_z + 2 * halo)
    origin = (
        lax.axis_index("gx") * width_x - halo,
        lax.axis_index("gy") * width_y - halo,
        lax.axis_index("gz") * width_z - halo,
    )
    total = (
        width_x * lax.axis_size("gx"),
        width_y * lax.axis_size("gy"),
        width_z * lax.axis_size("gz"),
    )

    rates = local_rates(slip_rate, taps, onsets)
    local_count = rates.shape[0]
    packed = jnp.concatenate([rates.reshape(-1), moment.T.reshape(-1)])
    lanes = -(-packed.shape[0] // 128) * 128
    packed = jnp.pad(packed, (0, lanes - packed.shape[0])).reshape(lanes // 128, 128)
    packed = gather_rows(packed).reshape(-1, lanes)
    rates_all = packed[:, : local_count * STEPS].reshape(-1, STEPS)
    moment_all = packed[:, local_count * STEPS : local_count * (STEPS + 6)].reshape(-1, 6)
    gathered = (rates_all[:, :, None] * moment_all[:, None, :]).reshape(rates_all.shape[0], -1)
    row_low = total[1] // 2 - 1
    row = cells[1] - row_low
    local_x = cells[0] - origin[0]
    local_z = cells[2] - origin[2]
    inside = (
        (row >= 0)
        & (row < 2)
        & (local_x >= 0)
        & (local_x < ext[0])
        & (local_z >= 0)
        & (local_z < ext[2])
    )
    row = jnp.where(inside, row, 2)
    local_x = jnp.where(inside, local_x, ext[0])
    local_z = jnp.where(inside, local_z, ext[2])
    strip = jnp.zeros((gathered.shape[1], 2, ext[0], ext[2]), jnp.float32)
    strip = strip.at[:, row, local_x, local_z].add(-STEP_TIME * gathered.T, mode="drop")
    across = lax.broadcasted_iota(jnp.int32, ext, 1) + origin[1]
    on_low = across == row_low
    on_high = across == row_low + 1

    keep = None
    for d in range(3):
        where = origin[d] + lax.broadcasted_iota(jnp.int32, ext, d)
        inside_d = (where >= 0) & (where < total[d])
        keep = inside_d if keep is None else keep & inside_d

    media = with_halo(jnp.stack([buoyancy, lame_lambda, shear_modulus]), halo)
    factor = STEP_TIME * media[0]
    lame_ext = media[1]
    shear_ext = media[2]
    stiffness = lame_ext + 2.0 * shear_ext

    def run_block(fields, rows_of_block, count):
        block = with_halo(fields, halo)
        velocity_now = [block[c] for c in range(3)]
        stress_now = [block[3 + c] for c in range(6)]
        for step in range(count):
            velocity_now = velocity_update(stress_now, velocity_now, factor)
            velocity_now = [jnp.where(keep, v, 0.0) for v in velocity_now]
            stress_now = stress_update(velocity_now, stress_now, lame_ext, shear_ext, stiffness)
            stress_now = [
                jnp.where(
                    keep,
                    stress_now[c]
                    + (
                        jnp.where(on_low, rows_of_block[step * 6 + c, 0][:, None, :], 0.0)
                        + jnp.where(on_high, rows_of_block[step * 6 + c, 1][:, None, :], 0.0)
                    ),
                    0.0,
                )
                for c in range(6)
            ]
        block = jnp.stack(velocity_now + stress_now)
        return block[:, halo : halo + width_x, halo : halo + width_y, halo : halo + width_z]

    blocks = STEPS // halo
    rest = STEPS - blocks * halo
    per_block = strip[: blocks * halo * 6].reshape((blocks, halo * 6) + strip.shape[1:])

    def body(index, fields):
        rows_of_block = lax.dynamic_index_in_dim(per_block, index, 0, keepdims=False)
        return run_block(fields, rows_of_block, halo)

    fields = jnp.concatenate([velocity, stress])
    if blocks:
        fields = run_block(fields, per_block[0], halo)
    fields = lax.fori_loop(1, blocks, body, fields)
    if rest:
        fields = run_block(fields, strip[blocks * halo * 6 :], rest)
    return (fields[:3], fields[3:])


def solution(mesh):
    placed = (
        P(None, "gx", "gy", "gz"),
        P(None, "gx", "gy", "gz"),
        P("gx", "gy", "gz"),
        P("gx", "gy", "gz"),
        P("gx", "gy", "gz"),
        P(("gx", "gy", "gz"), None),
        P(),
        P(None, ("gx", "gy", "gz")),
        P(),
        P(("gx", "gy", "gz")),
    )
    return jax.shard_map(
        on_device,
        mesh=mesh,
        in_specs=placed,
        out_specs=(P(None, "gx", "gy", "gz"), P(None, "gx", "gy", "gz")),
        check_vma=False,
    )
```

```python
import jax
import jax.numpy as jnp
from jax import lax
from jax.sharding import PartitionSpec as P

TAPS = 512
HOP = 64
STEPS = 16


STEP_TIME = 0.25
AXES = ("gx", "gy", "gz")
BLOCK = 4


def to_next(block, axis):
    count = lax.axis_size(axis)
    return lax.ppermute(block, axis, [(i, i + 1) for i in range(count - 1)])


def to_prev(block, axis):
    count = lax.axis_size(axis)
    return lax.ppermute(block, axis, [(i + 1, i) for i in range(count - 1)])


def with_halo(block, width):
    for axis, dim in (("gx", 1), ("gy", 2), ("gz", 3)):
        extent = block.shape[dim]
        low = to_next(lax.slice_in_dim(block, extent - width, extent, axis=dim), axis)
        high = to_prev(lax.slice_in_dim(block, 0, width, axis=dim), axis)
        block = jnp.concatenate([low, block, high], axis=dim)
    return block


def up(a, dim):
    edge = jnp.zeros_like(lax.slice_in_dim(a, 0, 1, axis=dim))
    return jnp.concatenate([lax.slice_in_dim(a, 1, a.shape[dim], axis=dim), edge], axis=dim)


def down(a, dim):
    edge = jnp.zeros_like(lax.slice_in_dim(a, 0, 1, axis=dim))
    return jnp.concatenate([edge, lax.slice_in_dim(a, 0, a.shape[dim] - 1, axis=dim)], axis=dim)


def forward(a, dim):
    return up(a, dim) - a


def backward(a, dim):
    return a - down(a, dim)


def velocity_update(stress, velocity, factor):
    sxx, syy, szz, sxy, sxz, syz = stress
    velocity_x = velocity[0] + factor * (forward(sxx, 0) + backward(sxy, 1) + backward(sxz, 2))
    velocity_y = velocity[1] + factor * (backward(sxy, 0) + forward(syy, 1) + backward(syz, 2))
    velocity_z = velocity[2] + factor * (backward(sxz, 0) + backward(syz, 1) + forward(szz, 2))
    return [velocity_x, velocity_y, velocity_z]


def stress_update(velocity, stress, lame_lambda, shear_modulus, stiffness):
    vx, vy, vz = velocity
    strain_x = backward(vx, 0)
    strain_y = backward(vy, 1)
    strain_z = backward(vz, 2)
    normal_x = stress[0] + STEP_TIME * (stiffness * strain_x + lame_lambda * (strain_y + strain_z))
    normal_y = stress[1] + STEP_TIME * (stiffness * strain_y + lame_lambda * (strain_x + strain_z))
    normal_z = stress[2] + STEP_TIME * (stiffness * strain_z + lame_lambda * (strain_x + strain_y))
    shear_xy = stress[3] + STEP_TIME * shear_modulus * (forward(vx, 1) + forward(vy, 0))
    shear_xz = stress[4] + STEP_TIME * shear_modulus * (forward(vx, 2) + forward(vz, 0))
    shear_yz = stress[5] + STEP_TIME * shear_modulus * (forward(vy, 2) + forward(vz, 1))
    return [normal_x, normal_y, normal_z, shear_xy, shear_xz, shear_yz]


def local_rates(slip_rate, taps, onsets):
    span = HOP * (STEPS - 1) + TAPS
    segments = jnp.concatenate(
        [
            lax.dynamic_slice(slip_rate, (f, onsets[f]), (1, span))
            for f in range(slip_rate.shape[0])
        ]
    )
    banded = jnp.stack(
        [jnp.pad(taps, (HOP * n, span - TAPS - HOP * n)) for n in range(STEPS)], axis=1
    )
    return jnp.dot(segments, banded, preferred_element_type=jnp.float32)


def gather_rows(rows):
    for axis in ("gz", "gy", "gx"):
        count = lax.axis_size(axis)
        if count & (count - 1):
            rows = lax.all_gather(rows, axis, axis=0, tiled=True)
            continue
        index = lax.axis_index(axis)
        stride = 1
        while stride < count:
            radix = 4 if count % (stride * 4) == 0 else 2
            place = (index // stride) % radix
            pieces = [rows]
            for shift in range(1, radix):
                pairs = []
                for source in range(count):
                    at = (source // stride) % radix
                    pairs.append((source, source + ((at - shift) % radix - at) * stride))
                pieces.append(lax.ppermute(rows, axis, pairs))
            order = (jnp.arange(radix) - place) % radix
            rows = jnp.stack(pieces)[order].reshape(-1, rows.shape[-1])
            stride *= radix
    return rows


def on_device(
    velocity, stress, buoyancy, lame_lambda, shear_modulus, slip_rate, taps, moment, cells, onsets
):
    width_x, width_y, width_z = buoyancy.shape
    halo = min(BLOCK, width_x, width_y, width_z, STEPS)
    ext = (width_x + 2 * halo, width_y + 2 * halo, width_z + 2 * halo)
    origin = (
        lax.axis_index("gx") * width_x - halo,
        lax.axis_index("gy") * width_y - halo,
        lax.axis_index("gz") * width_z - halo,
    )
    total = (
        width_x * lax.axis_size("gx"),
        width_y * lax.axis_size("gy"),
        width_z * lax.axis_size("gz"),
    )

    rates = local_rates(slip_rate, taps, onsets)
    local_count = rates.shape[0]
    packed = jnp.concatenate([rates.reshape(-1), moment.T.reshape(-1)])
    lanes = -(-packed.shape[0] // 128) * 128
    packed = jnp.pad(packed, (0, lanes - packed.shape[0])).reshape(lanes // 128, 128)
    packed = gather_rows(packed).reshape(-1, lanes)
    rates_all = packed[:, : local_count * STEPS].reshape(-1, STEPS)
    moment_all = packed[:, local_count * STEPS : local_count * (STEPS + 6)].reshape(-1, 6)
    gathered = (rates_all[:, :, None] * moment_all[:, None, :]).reshape(rates_all.shape[0], -1)
    row_low = total[1] // 2 - 1
    row = cells[1] - row_low
    local_x = cells[0] - origin[0]
    local_z = cells[2] - origin[2]
    inside = (
        (row >= 0)
        & (row < 2)
        & (local_x >= 0)
        & (local_x < ext[0])
        & (local_z >= 0)
        & (local_z < ext[2])
    )
    row = jnp.where(inside, row, 2)
    local_x = jnp.where(inside, local_x, ext[0])
    local_z = jnp.where(inside, local_z, ext[2])
    strip = jnp.zeros((gathered.shape[1], 2, ext[0], ext[2]), jnp.float32)
    strip = strip.at[:, row, local_x, local_z].add(-STEP_TIME * gathered.T, mode="drop")
    across = lax.broadcasted_iota(jnp.int32, ext, 1) + origin[1]
    on_low = across == row_low
    on_high = across == row_low + 1

    keep = None
    for d in range(3):
        where = origin[d] + lax.broadcasted_iota(jnp.int32, ext, d)
        inside_d = (where >= 0) & (where < total[d])
        keep = inside_d if keep is None else keep & inside_d

    media = with_halo(jnp.stack([buoyancy, lame_lambda, shear_modulus]), halo)
    factor = STEP_TIME * media[0]
    lame_ext = media[1]
    shear_ext = media[2]
    stiffness = lame_ext + 2.0 * shear_ext

    def run_block(fields, rows_of_block, count):
        block = with_halo(fields, halo)
        velocity_now = [block[c] for c in range(3)]
        stress_now = [block[3 + c] for c in range(6)]
        added = jnp.where(on_low, rows_of_block[:, 0][:, :, None, :], 0.0) + jnp.where(
            on_high, rows_of_block[:, 1][:, :, None, :], 0.0
        )
        for step in range(count):
            velocity_now = velocity_update(stress_now, velocity_now, factor)
            velocity_now = [jnp.where(keep, v, 0.0) for v in velocity_now]
            stress_now = stress_update(velocity_now, stress_now, lame_ext, shear_ext, stiffness)
            stress_now = [
                jnp.where(keep, stress_now[c] + added[step * 6 + c], 0.0) for c in range(6)
            ]
        block = jnp.stack(velocity_now + stress_now)
        return block[:, halo : halo + width_x, halo : halo + width_y, halo : halo + width_z]

    blocks = STEPS // halo
    rest = STEPS - blocks * halo
    per_block = strip[: blocks * halo * 6].reshape((blocks, halo * 6) + strip.shape[1:])

    def body(index, fields):
        rows_of_block = lax.dynamic_index_in_dim(per_block, index, 0, keepdims=False)
        return run_block(fields, rows_of_block, halo)

    fields = lax.fori_loop(0, blocks, body, jnp.concatenate([velocity, stress]))
    if rest:
        fields = run_block(fields, strip[blocks * halo * 6 :], rest)
    return (fields[:3], fields[3:])


def solution(mesh):
    placed = (
        P(None, "gx", "gy", "gz"),
        P(None, "gx", "gy", "gz"),
        P("gx", "gy", "gz"),
        P("gx", "gy", "gz"),
        P("gx", "gy", "gz"),
        P(("gx", "gy", "gz"), None),
        P(),
        P(None, ("gx", "gy", "gz")),
        P(),
        P(("gx", "gy", "gz")),
    )
    return jax.shard_map(
        on_device,
        mesh=mesh,
        in_specs=placed,
        out_specs=(P(None, "gx", "gy", "gz"), P(None, "gx", "gy", "gz")),
        check_vma=False,
    )
```
